512 devices in a mesh: shard: 128 (over z, y, core), tensor: 4 (over x).
Axes of the slice: x: 4, y: 8, z: 8, core: 2. Of those that a mesh axis runs over, the one named last changes fastest.
Arguments:
- grad_query: bfloat16 [4, 2048, 2048], P(None, 'shard', 'tensor'), may hold values from -300 to 300, as said below
- grad_key: bfloat16 [4, 2048, 2048], P(None, 'shard', 'tensor'), may hold values from -300 to 300
- grad_value: bfloat16 [4, 2048, 2048], P(None, 'shard', 'tensor'), may hold values from -300 to 300
- grad_output: bfloat16 [4, 2048, 2048], P(None, 'shard', 'tensor'), may hold values from -300 to 300
- grad_gate: bfloat16 [4, 2048, 5120], P(None, 'shard', 'tensor'), may hold values from -300 to 300
- grad_linear: bfloat16 [4, 2048, 5120], P(None, 'shard', 'tensor'), may hold values from -300 to 300
- grad_down: bfloat16 [4, 2048, 5120], P(None, 'shard', 'tensor'), may hold values from -300 to 300
- grad_norms: bfloat16 [4, 4, 2, 2048], P(None, 'tensor', None, 'shard'), may hold values from -24 to 24
- master_flat: float32 [128, 4, 94208], P('shard', 'tensor'), may hold values from -4 to 4
- first_moment: float32 [128, 4, 94208], P('shard', 'tensor'), may hold values from -3 to 3
- second_moment: float32 [128, 4, 94208], P('shard', 'tensor'), may hold values from 0.05 to 1
- gain_master: float32 [2, 2048], P(None, 'shard'), may hold values from 0.5 to 1.5
- gain_first: float32 [2, 2048], P(None, 'shard'), may hold values from -3 to 3
- gain_second: float32 [2, 2048], P(None, 'shard'), may hold values from 0.05 to 1
Outputs:
- new_master: float32 [128, 4, 94208], P('shard', 'tensor')
- new_first: float32 [128, 4, 94208], P('shard', 'tensor')
- new_second: float32 [128, 4, 94208], P('shard', 'tensor')
- new_gains: float32 [2, 2048], P(None, 'shard')
- new_gain_first: float32 [2, 2048], P(None, 'shard')
- new_gain_second: float32 [2, 2048], P(None, 'shard')
- copy_query: bfloat16 [2048, 2048], P('shard', 'tensor')
- copy_key: bfloat16 [2048, 2048], P('shard', 'tensor')
- copy_value: bfloat16 [2048, 2048], P('shard', 'tensor')
- copy_output: bfloat16 [2048, 2048], P('shard', 'tensor')
- copy_gate: bfloat16 [2048, 5120], P('shard', 'tensor')
- copy_linear: bfloat16 [2048, 5120], P('shard', 'tensor')
- copy_down: bfloat16 [2048, 5120], P('shard', 'tensor')
- copy_gains: bfloat16 [2, 2048], P(None, 'shard')
- grad_rms: float32 [], replicated
The draws below stay inside these ranges and needn't reach their ends.
Inputs may be any that keep to these rules, and one draw needn't show every extreme that they name: `grad_query`: grad_rms is above 0.5 in every draw, so the clip factor is below one.
All inputs are finite; a program needn't handle non-finite values.
Results may differ from the reference program's by a relative error of at most 0.00045.
Values may be sent and summed in bfloat16 or wider, within the bound.
No kernel may reach another device: no remote copies, remote signals or barrier semaphores. Data moves between devices by JAX's collectives and lax.ppermute only.
A program may use at most 64 MiB of HBM per device.

```python
import math
import jax
import jax.numpy as jnp
from jax import lax

D = 2048
INNER = 2048
FF = 5120
MB = 4
STEP = 20
FLATW = 46
FLAT = 94208
COUNT = 48238592
N_SHARD = 128
N_TENSOR = 4


def spread_levels(key, count):
    subkeys = jax.random.split(key, 2)
    ranking = jax.random.permutation(subkeys[0], count).astype(jnp.float32)
    jitter = jax.random.uniform(subkeys[1], (count,))
    return (ranking + jitter) / count


def quarter_levels(key):
    return spread_levels(jax.random.fold_in(key, 99), 28)


def gradient_draw(key, columns, group_index):
    levels = quarter_levels(key)[4 * group_index:4 * group_index + 4]
    subkeys = jax.random.split(jax.random.fold_in(key, 11 + group_index), 7)
    head_count = columns // 64
    row_index = jnp.arange(D, dtype=jnp.float32)
    row_rise = jnp.sqrt(1.0 + 2.0 * row_index / (D - 1))
    row_profile = row_rise[None, :] * 10.0 ** (1.5 * jax.random.uniform(subkeys[0], (head_count, D)))
    head_scale = 10.0 ** (1.5 * spread_levels(subkeys[1], head_count))
    column_scale = 10.0 ** (0.3 * jax.random.uniform(subkeys[2], (columns,)))
    quarter_scale = 10.0 ** (1.5 * levels)
    column_total = column_scale * jnp.repeat(head_scale, 64) * jnp.repeat(quarter_scale, columns // 4)
    scales = jnp.transpose(jnp.repeat(row_profile, 64, axis=0)) * column_total[None, :]
    common = jnp.clip(jax.random.normal(subkeys[5], (1, D, columns)), -4.0, 4.0)
    private = jnp.clip(jax.random.normal(subkeys[6], (MB, D, columns)), -4.0, 4.0)
    values = (0.8 * common + 0.6 * private) * scales * 0.00048
    return values.astype(jnp.bfloat16)


def draw_grad_query(key, part):
    return gradient_draw(key, INNER, 0)


def draw_grad_key(key, part):
    return gradient_draw(key, INNER, 1)


def draw_grad_value(key, part):
    return gradient_draw(key, INNER, 2)


def draw_grad_output(key, part):
    return gradient_draw(key, INNER, 3)


def draw_grad_gate(key, part):
    return gradient_draw(key, FF, 4)


def draw_grad_linear(key, part):
    return gradient_draw(key, FF, 5)


def draw_grad_down(key, part):
    return gradient_draw(key, FF, 6)


def steps_of(own_key, dims, cuts, least, largest):
    def one(position, shards_of):
        draws = jax.random.uniform(jax.random.fold_in(jax.random.fold_in(own_key, 6), position), (shards_of,), jnp.float32, least / len(cuts), largest / len(cuts))
        return jnp.repeat(jnp.exp(draws), dims[position] // shards_of).reshape((-1,) + (1,) * (len(dims) - position - 1))

    level = one(*cuts[0])
    for cut in cuts[1:]:
        level = level * one(*cut)
    return level


def normal_values(key, shape, deviation, most, shards=(), kind=jnp.bfloat16):
    level = steps_of(key, shape, shards, -0.22, 0.18) if shards else 1.0
    drawn = jax.random.normal(key, shape, jnp.float32) * deviation * level
    return jnp.minimum(jnp.maximum(drawn, -most), most).astype(kind)


def setup_inputs(seed: int = 0) -> dict:
    splits = jax.random.split(jax.random.key(seed), 15)
    return {
        "grad_query": draw_grad_query(jax.random.fold_in(splits[14], 71), 0),
        "grad_key": draw_grad_key(jax.random.fold_in(splits[14], 71), 0),
        "grad_value": draw_grad_value(jax.random.fold_in(splits[14], 71), 0),
        "grad_output": draw_grad_output(jax.random.fold_in(splits[14], 71), 0),
        "grad_gate": draw_grad_gate(jax.random.fold_in(splits[14], 71), 0),
        "grad_linear": draw_grad_linear(jax.random.fold_in(splits[14], 71), 0),
        "grad_down": draw_grad_down(jax.random.fold_in(splits[14], 71), 0),
        "grad_norms": normal_values(splits[7], (MB, N_TENSOR, 2, D), 4.0, 24.0, ((1, 4), (3, 128))),
        "master_flat": normal_values(splits[8], (N_SHARD, N_TENSOR, FLAT), 0.5, 4.0, ((0, 128), (1, 4)), jnp.float32),
        "first_moment": normal_values(splits[9], (N_SHARD, N_TENSOR, FLAT), 0.3, 3.0, ((0, 128), (1, 4)), jnp.float32),
        "second_moment": jnp.clip(jnp.exp(math.log(1.0) - 2.9957323 * jax.random.uniform(splits[10], (N_SHARD, N_TENSOR, FLAT), jnp.float32) ** steps_of(splits[10], (N_SHARD, N_TENSOR, FLAT), ((0, 128), (1, 4)), -0.2, 0.2)), 0.05, 1.0),
        "gain_master": jnp.clip(1.0 + 0.1 * jax.random.normal(splits[11], (2, D), jnp.float32), 0.5, 1.5),
        "gain_first": normal_values(splits[12], (2, D), 0.3, 3.0, ((1, 128),), jnp.float32),
        "gain_second": jnp.clip(jnp.exp(math.log(1.0) - 2.9957323 * jax.random.uniform(splits[13], (2, D), jnp.float32) ** steps_of(splits[13], (2, D), ((1, 128),), -0.2, 0.2)), 0.05, 1.0),
    }


BETA1 = 0.9
BETA2 = 0.95
EPSILON = 1e-08
LRATE = 0.2
WDECAY = 2.5
CLIP_RMS = 0.5

def group_columns():
    return [INNER, INNER, INNER, INNER, FF, FF, FF]

def unflatten(flat_array):
    regrouped = flat_array.reshape(N_SHARD, N_TENSOR, D, FLATW)
    result = []
    offset = 0
    for column_count in group_columns():
        group_width = column_count // (N_SHARD * N_TENSOR)
        section = regrouped[:, :, :, offset:offset + group_width]
        result.append(jnp.transpose(section, (2, 1, 0, 3)).reshape(D, column_count))
        offset = offset + group_width
    return result

def flatten(matrices):
    sections = []
    for matrix, column_count in zip(matrices, group_columns()):
        group_width = column_count // (N_SHARD * N_TENSOR)
        sections.append(jnp.transpose(matrix.reshape(D, N_TENSOR, N_SHARD, group_width), (2, 1, 0, 3)))
    return jnp.concatenate(sections, axis=3).reshape(N_SHARD, N_TENSOR, FLAT)

def adamw(weight, gradient, moment_one, moment_two, decay_rate, factor):
    clipped = gradient * factor
    moment_one_new = BETA1 * moment_one + (1.0 - BETA1) * clipped
    moment_two_new = BETA2 * moment_two + (1.0 - BETA2) * clipped * clipped
    update = moment_one_new / (1.0 - BETA1 ** STEP) / (jnp.sqrt(moment_two_new / (1.0 - BETA2 ** STEP)) + EPSILON)
    return (weight - LRATE * (update + decay_rate * weight), moment_one_new, moment_two_new)

def reference(grad_query, grad_key, grad_value, grad_output, grad_gate, grad_linear, grad_down, grad_norms, master_flat, first_moment, second_moment, gain_master, gain_first, gain_second):
    gradients = [grad_query, grad_key, grad_value, grad_output, grad_gate, grad_linear, grad_down]
    group_means = [lax.optimization_barrier(jnp.sum(matrix.astype(jnp.float32), axis=0)) * (1.0 / MB) for matrix in gradients]
    gain_grad = lax.optimization_barrier(jnp.sum(grad_norms.astype(jnp.float32), axis=(0, 1))) * (1.0 / MB)
    square_total = jnp.sum(gain_grad * gain_grad)
    for averaged in group_means:
        square_total = square_total + jnp.sum(averaged * averaged)
    grad_rms = jnp.sqrt(square_total / COUNT)
    factor = jnp.minimum(1.0, CLIP_RMS / grad_rms)
    masters = unflatten(master_flat)
    firsts = unflatten(first_moment)
    seconds = unflatten(second_moment)
    new_weights = []
    new_firsts = []
    new_seconds = []
    for weight, averaged, moment_one, moment_two in zip(masters, group_means, firsts, seconds):
        weight_new, one_new, two_new = adamw(weight, averaged, moment_one, moment_two, WDECAY, factor)
        new_weights.append(weight_new)
        new_firsts.append(one_new)
        new_seconds.append(two_new)
    gains_new, gain_one, gain_two = adamw(gain_master, gain_grad, gain_first, gain_second, 0.0, factor)
    copies = [weight.astype(jnp.bfloat16) for weight in new_weights]
    return (flatten(new_weights), flatten(new_firsts), flatten(new_seconds), gains_new, gain_one, gain_two, copies[0], copies[1], copies[2], copies[3], copies[4], copies[5], copies[6], gains_new.astype(jnp.bfloat16), grad_rms)
```

```python
import jax
import jax.numpy as jnp
from jax import lax
from jax.sharding import PartitionSpec as P

MB = 4
STEP = 20
COUNT = 48238592


BETA1 = 0.9
BETA2 = 0.95
EPSILON = 1e-08
LRATE = 0.2
WDECAY = 2.5
CLIP_RMS = 0.5


def adamw(weight, gradient, moment_one, moment_two, decay_rate, factor):
    clipped = gradient * factor
    moment_one_new = BETA1 * moment_one + (1.0 - BETA1) * clipped
    moment_two_new = BETA2 * moment_two + (1.0 - BETA2) * clipped * clipped
    update = (
        moment_one_new
        / (1.0 - BETA1**STEP)
        / (jnp.sqrt(moment_two_new / (1.0 - BETA2**STEP)) + EPSILON)
    )
    return (weight - LRATE * (update + decay_rate * weight), moment_one_new, moment_two_new)


def mean_block(matrix):
    return jnp.sum(matrix.astype(jnp.float32), axis=0) * (1.0 / MB)


def by_destination(group_means, shard_count):
    rows = group_means[0].shape[0]
    sections = [
        matrix.reshape(rows, shard_count, matrix.shape[-1] // shard_count) for matrix in group_means
    ]
    joined = jnp.concatenate(sections, axis=-1)
    return jnp.transpose(joined, (1, 0, 2)).reshape(shard_count, -1)


def shards(
    grad_query,
    grad_key,
    grad_value,
    grad_output,
    grad_gate,
    grad_linear,
    grad_down,
    grad_norms,
    master_flat,
    first_moment,
    second_moment,
    gain_master,
    gain_first,
    gain_second,
):
    blocks = [grad_query, grad_key, grad_value, grad_output, grad_gate, grad_linear, grad_down]
    shard_count = lax.axis_size("shard")
    rows = grad_query.shape[1]
    group_widths = [matrix.shape[2] // shard_count for matrix in blocks]
    flat_width = sum(group_widths)

    group_means = [mean_block(matrix) for matrix in blocks]
    block_square = jnp.sum(group_means[0] * group_means[0])
    for averaged in group_means[1:]:
        block_square = block_square + jnp.sum(averaged * averaged)

    gain_local = jnp.sum(grad_norms.astype(jnp.float32), axis=(0, 1))
    gain_size = gain_local.size
    summed = lax.psum(jnp.concatenate([gain_local.reshape(-1), block_square.reshape(1)]), "tensor")
    gain_grad = summed[:gain_size].reshape(gain_local.shape) * (1.0 / MB)
    shard_square = summed[gain_size] + jnp.sum(gain_grad * gain_grad)

    payload = by_destination(group_means, shard_count)
    payload = jnp.concatenate(
        [payload, jnp.broadcast_to(shard_square, (shard_count, 1))], axis=1
    )
    received = lax.all_to_all(payload, "shard", split_axis=0, concat_axis=0, tiled=True)
    square_total = jnp.sum(received[:, rows * flat_width])
    grad_flat = received[:, : rows * flat_width].reshape(-1)

    grad_rms = jnp.sqrt(square_total / COUNT)
    factor = jnp.minimum(1.0, CLIP_RMS / grad_rms)
    weights, firsts, seconds = adamw(
        master_flat.reshape(-1),
        grad_flat,
        first_moment.reshape(-1),
        second_moment.reshape(-1),
        WDECAY,
        factor,
    )
    gains_new, gain_one, gain_two = adamw(
        gain_master, gain_grad, gain_first, gain_second, 0.0, factor
    )

    lowered = weights.astype(jnp.bfloat16).reshape(shard_count, rows * flat_width)
    returned = lax.all_to_all(lowered, "shard", split_axis=0, concat_axis=0, tiled=True)
    returned = returned.reshape(shard_count, rows, flat_width)
    copies = []
    offset = 0
    for group_width in group_widths:
        section = returned[:, :, offset : offset + group_width]
        copies.append(jnp.transpose(section, (1, 0, 2)).reshape(rows, shard_count * group_width))
        offset = offset + group_width
    gain_copy = gains_new.astype(jnp.bfloat16)
    return (
        weights.reshape(master_flat.shape),
        firsts.reshape(master_flat.shape),
        seconds.reshape(master_flat.shape),
        gains_new,
        gain_one,
        gain_two,
        copies[0],
        copies[1],
        copies[2],
        copies[3],
        copies[4],
        copies[5],
        copies[6],
        gain_copy,
        grad_rms,
    )


def solution(mesh):
    return jax.shard_map(
        shards,
        mesh=mesh,
        in_specs=(
            P(None, "shard", "tensor"),
            P(None, "shard", "tensor"),
            P(None, "shard", "tensor"),
            P(None, "shard", "tensor"),
            P(None, "shard", "tensor"),
            P(None, "shard", "tensor"),
            P(None, "shard", "tensor"),
            P(None, "tensor", None, "shard"),
            P("shard", "tensor", None),
            P("shard", "tensor", None),
            P("shard", "tensor", None),
            P(None, "shard"),
            P(None, "shard"),
            P(None, "shard"),
        ),
        out_specs=(
            P("shard", "tensor", None),
            P("shard", "tensor", None),
            P("shard", "tensor", None),
            P(None, "shard"),
            P(None, "shard"),
            P(None, "shard"),
            P("shard", "tensor"),
            P("shard", "tensor"),
            P("shard", "tensor"),
            P("shard", "tensor"),
            P("shard", "tensor"),
            P("shard", "tensor"),
            P("shard", "tensor"),
            P(None, "shard"),
            P(),
        ),
        check_vma=False,
    )
```

```python
import jax
import jax.numpy as jnp
from jax import lax
from jax.sharding import PartitionSpec as P

MB = 4
STEP = 20
COUNT = 48238592


BETA1 = 0.9
BETA2 = 0.95
EPSILON = 1e-08
LRATE = 0.2
WDECAY = 2.5
CLIP_RMS = 0.5


def adamw(weight, gradient, moment_one, moment_two, decay_rate, factor):
    clipped = gradient * factor
    moment_one_new = BETA1 * moment_one + (1.0 - BETA1) * clipped
    moment_two_new = BETA2 * moment_two + (1.0 - BETA2) * clipped * clipped
    update = (
        moment_one_new
        / (1.0 - BETA1**STEP)
        / (jnp.sqrt(moment_two_new / (1.0 - BETA2**STEP)) + EPSILON)
    )
    return (weight - LRATE * (update + decay_rate * weight), moment_one_new, moment_two_new)


def mean_block(matrix):
    return jnp.sum(matrix.astype(jnp.float32), axis=0) * (1.0 / MB)


def by_destination(group_means, shard_count):
    rows = group_means[0].shape[0]
    sections = [
        matrix.reshape(rows, shard_count, matrix.shape[-1] // shard_count) for matrix in group_means
    ]
    joined = jnp.concatenate(sections, axis=-1)
    return jnp.transpose(joined, (1, 0, 2)).reshape(shard_count, -1)


def tensor_sum(value):
    count = lax.axis_size("tensor")
    if count & (count - 1):
        return lax.psum(value, "tensor")
    step = 1
    while step < count:
        pairs = [(index, index ^ step) for index in range(count)]
        value = value + lax.ppermute(value, "tensor", pairs)
        step = step * 2
    return value


def shards(
    grad_query,
    grad_key,
    grad_value,
    grad_output,
    grad_gate,
    grad_linear,
    grad_down,
    grad_norms,
    master_flat,
    first_moment,
    second_moment,
    gain_master,
    gain_first,
    gain_second,
):
    blocks = [grad_query, grad_key, grad_value, grad_output, grad_gate, grad_linear, grad_down]
    shard_count = lax.axis_size("shard")
    rows = grad_query.shape[1]
    group_widths = [matrix.shape[2] // shard_count for matrix in blocks]
    flat_width = sum(group_widths)

    group_means = [mean_block(matrix) for matrix in blocks]
    lanes = 128
    block_square = jnp.sum((group_means[0] * group_means[0]).reshape(-1, lanes), axis=0)
    for averaged in group_means[1:]:
        block_square = block_square + jnp.sum((averaged * averaged).reshape(-1, lanes), axis=0)

    gain_local = jnp.sum(grad_norms.astype(jnp.float32), axis=(0, 1))
    gain_size = gain_local.size
    summed = tensor_sum(jnp.concatenate([gain_local.reshape(-1), block_square]))
    gain_grad = summed[:gain_size].reshape(gain_local.shape) * (1.0 / MB)
    shard_square = jnp.sum(
        jnp.concatenate([summed[gain_size:], (gain_grad * gain_grad).reshape(-1)])
    )

    payload = by_destination(group_means, shard_count)
    payload = jnp.concatenate(
        [payload, jnp.broadcast_to(shard_square, (shard_count, 1))], axis=1
    )
    received = lax.all_to_all(payload, "shard", split_axis=0, concat_axis=0, tiled=True)
    square_total = jnp.sum(received[:, rows * flat_width])
    grad_flat = received[:, : rows * flat_width].reshape(-1)

    grad_rms = jnp.sqrt(square_total / COUNT)
    factor = jnp.minimum(1.0, CLIP_RMS / grad_rms)
    weights, firsts, seconds = adamw(
        master_flat.reshape(-1),
        grad_flat,
        first_moment.reshape(-1),
        second_moment.reshape(-1),
        WDECAY,
        factor,
    )
    gains_new, gain_one, gain_two = adamw(
        gain_master, gain_grad, gain_first, gain_second, 0.0, factor
    )

    lowered = weights.astype(jnp.bfloat16).reshape(shard_count, rows * flat_width)
    returned = lax.all_to_all(lowered, "shard", split_axis=0, concat_axis=0, tiled=True)
    returned = returned.reshape(shard_count, rows, flat_width)
    copies = []
    offset = 0
    for group_width in group_widths:
        section = returned[:, :, offset : offset + group_width]
        copies.append(jnp.transpose(section, (1, 0, 2)).reshape(rows, shard_count * group_width))
        offset = offset + group_width
    gain_copy = gains_new.astype(jnp.bfloat16)
    return (
        weights.reshape(master_flat.shape),
        firsts.reshape(master_flat.shape),
        seconds.reshape(master_flat.shape),
        gains_new,
        gain_one,
        gain_two,
        copies[0],
        copies[1],
        copies[2],
        copies[3],
        copies[4],
        copies[5],
        copies[6],
        gain_copy,
        grad_rms,
    )


def solution(mesh):
    return jax.shard_map(
        shards,
        mesh=mesh,
        in_specs=(
            P(None, "shard", "tensor"),
            P(None, "shard", "tensor"),
            P(None, "shard", "tensor"),
            P(None, "shard", "tensor"),
            P(None, "shard", "tensor"),
            P(None, "shard", "tensor"),
            P(None, "shard", "tensor"),
            P(None, "tensor", None, "shard"),
            P("shard", "tensor", None),
            P("shard", "tensor", None),
            P("shard", "tensor", None),
            P(None, "shard"),
            P(None, "shard"),
            P(None, "shard"),
        ),
        out_specs=(
            P("shard", "tensor", None),
            P("shard", "tensor", None),
            P("shard", "tensor", None),
            P(None, "shard"),
            P(None, "shard"),
            P(None, "shard"),
            P("shard", "tensor"),
            P("shard", "tensor"),
            P("shard", "tensor"),
            P("shard", "tensor"),
            P("shard", "tensor"),
            P("shard", "tensor"),
            P("shard", "tensor"),
            P(None, "shard"),
            P(),
        ),
        check_vma=False,
    )
```

```python
import jax
import jax.numpy as jnp
from jax import lax
from jax.sharding import PartitionSpec as P

MB = 4
STEP = 20
COUNT = 48238592


BETA1 = 0.9
BETA2 = 0.95
EPSILON = 1e-08
LRATE = 0.2
WDECAY = 2.5
CLIP_RMS = 0.5


def adamw(weight, gradient, moment_one, moment_two, decay_rate, factor):
    clipped = gradient * factor
    moment_one_new = BETA1 * moment_one + (1.0 - BETA1) * clipped
    moment_two_new = BETA2 * moment_two + (1.0 - BETA2) * clipped * clipped
    update = (
        moment_one_new
        / (1.0 - BETA1**STEP)
        / (jnp.sqrt(moment_two_new / (1.0 - BETA2**STEP)) + EPSILON)
    )
    return (weight - LRATE * (update + decay_rate * weight), moment_one_new, moment_two_new)


def mean_block(matrix):
    return jnp.sum(matrix.astype(jnp.float32), axis=0) * (1.0 / MB)


def by_destination(group_means, shard_count):
    rows = group_means[0].shape[0]
    sections = [
        matrix.reshape(rows, shard_count, matrix.shape[-1] // shard_count) for matrix in group_means
    ]
    joined = jnp.concatenate(sections, axis=-1)
    return jnp.transpose(joined, (1, 0, 2)).reshape(shard_count, -1)


def tensor_sum(value):
    count = lax.axis_size("tensor")
    if count == 4:
        masks = (1, 3)
    elif count & (count - 1) == 0:
        masks = tuple(1 << bit for bit in range(count.bit_length() - 1))
    else:
        return lax.psum(value, "tensor")
    for mask in masks:
        pairs = [(index, index ^ mask) for index in range(count)]
        value = value + lax.ppermute(value, "tensor", pairs)
    return value


def shards(
    grad_query,
    grad_key,
    grad_value,
    grad_output,
    grad_gate,
    grad_linear,
    grad_down,
    grad_norms,
    master_flat,
    first_moment,
    second_moment,
    gain_master,
    gain_first,
    gain_second,
):
    blocks = [grad_query, grad_key, grad_value, grad_output, grad_gate, grad_linear, grad_down]
    shard_count = lax.axis_size("shard")
    rows = grad_query.shape[1]
    group_widths = [matrix.shape[2] // shard_count for matrix in blocks]
    flat_width = sum(group_widths)

    group_means = [mean_block(matrix) for matrix in blocks]
    lanes = 128
    block_square = jnp.sum((group_means[0] * group_means[0]).reshape(-1, lanes), axis=0)
    for averaged in group_means[1:]:
        block_square = block_square + jnp.sum((averaged * averaged).reshape(-1, lanes), axis=0)

    gain_local = jnp.sum(grad_norms.astype(jnp.float32), axis=(0, 1))
    gain_size = gain_local.size
    summed = tensor_sum(jnp.concatenate([gain_local.reshape(-1), block_square]))
    gain_grad = summed[:gain_size].reshape(gain_local.shape) * (1.0 / MB)
    gain_square = (gain_grad * gain_grad).reshape(-1)
    shard_square = jnp.sum(
        summed[gain_size:] + jnp.pad(gain_square, (0, lanes - gain_size))
    )

    payload = by_destination(group_means, shard_count)
    payload = jnp.concatenate(
        [payload, jnp.broadcast_to(shard_square, (shard_count, 1))], axis=1
    )
    received = lax.all_to_all(payload, "shard", split_axis=0, concat_axis=0, tiled=True)
    square_total = jnp.sum(received[:, rows * flat_width])
    grad_flat = received[:, : rows * flat_width].reshape(-1)

    grad_rms = jnp.sqrt(square_total / COUNT)
    factor = jnp.minimum(1.0, CLIP_RMS / grad_rms)
    weights, firsts, seconds = adamw(
        master_flat.reshape(-1),
        grad_flat,
        first_moment.reshape(-1),
        second_moment.reshape(-1),
        WDECAY,
        factor,
    )
    gains_new, gain_one, gain_two = adamw(
        gain_master, gain_grad, gain_first, gain_second, 0.0, factor
    )

    lowered = weights.astype(jnp.bfloat16).reshape(shard_count, rows * flat_width)
    returned = lax.all_to_all(lowered, "shard", split_axis=0, concat_axis=0, tiled=True)
    returned = returned.reshape(shard_count, rows, flat_width)
    copies = []
    offset = 0
    for group_width in group_widths:
        section = returned[:, :, offset : offset + group_width]
        copies.append(jnp.transpose(section, (1, 0, 2)).reshape(rows, shard_count * group_width))
        offset = offset + group_width
    gain_copy = gains_new.astype(jnp.bfloat16)
    return (
        weights.reshape(master_flat.shape),
        firsts.reshape(master_flat.shape),
        seconds.reshape(master_flat.shape),
        gains_new,
        gain_one,
        gain_two,
        copies[0],
        copies[1],
        copies[2],
        copies[3],
        copies[4],
        copies[5],
        copies[6],
        gain_copy,
        grad_rms,
    )


def solution(mesh):
    return jax.shard_map(
        shards,
        mesh=mesh,
        in_specs=(
            P(None, "shard", "tensor"),
            P(None, "shard", "tensor"),
            P(None, "shard", "tensor"),
            P(None, "shard", "tensor"),
            P(None, "shard", "tensor"),
            P(None, "shard", "tensor"),
            P(None, "shard", "tensor"),
            P(None, "tensor", None, "shard"),
            P("shard", "tensor", None),
            P("shard", "tensor", None),
            P("shard", "tensor", None),
            P(None, "shard"),
            P(None, "shard"),
            P(None, "shard"),
        ),
        out_specs=(
            P("shard", "tensor", None),
            P("shard", "tensor", None),
            P("shard", "tensor", None),
            P(None, "shard"),
            P(None, "shard"),
            P(None, "shard"),
            P("shard", "tensor"),
            P("shard", "tensor"),
            P("shard", "tensor"),
            P("shard", "tensor"),
            P("shard", "tensor"),
            P("shard", "tensor"),
            P("shard", "tensor"),
            P(None, "shard"),
            P(),
        ),
        check_vma=False,
    )
```

```python
import jax
import jax.numpy as jnp
from jax import lax
from jax.experimental import pallas as pl
from jax.experimental.pallas import tpu as pltpu
from jax.sharding import PartitionSpec as P

MB = 4
STEP = 20
COUNT = 48238592


BETA1 = 0.9
BETA2 = 0.95
EPSILON = 1e-08
LRATE = 0.2
WDECAY = 2.5
CLIP_RMS = 0.5


def adamw(weight, gradient, moment_one, moment_two, decay_rate, factor):
    clipped = gradient * factor
    moment_one_new = BETA1 * moment_one + (1.0 - BETA1) * clipped
    moment_two_new = BETA2 * moment_two + (1.0 - BETA2) * clipped * clipped
    update = (
        moment_one_new
        / (1.0 - BETA1**STEP)
        / (jnp.sqrt(moment_two_new / (1.0 - BETA2**STEP)) + EPSILON)
    )
    return (weight - LRATE * (update + decay_rate * weight), moment_one_new, moment_two_new)


def mean_block(matrix):
    return jnp.sum(matrix.astype(jnp.float32), axis=0) * (1.0 / MB)


def means_kernel(*refs):
    count = (len(refs) - 1) // 2
    grads, means, square_ref = refs[:count], refs[count : 2 * count], refs[2 * count]
    lanes = square_ref.shape[-1]
    square = jnp.zeros((grads[0].shape[1], lanes), jnp.float32)
    for grad_ref, mean_ref in zip(grads, means):
        total = grad_ref[0].astype(jnp.float32)
        for batch in range(1, grad_ref.shape[0]):
            total = total + grad_ref[batch].astype(jnp.float32)
        averaged = total * (1.0 / MB)
        mean_ref[...] = averaged
        for start in range(0, averaged.shape[1], lanes):
            part = averaged[:, start : start + lanes]
            square = square + part * part
    square_ref[...] = jnp.sum(square, axis=0, keepdims=True)


def means_and_squares(blocks, lanes):
    rows = blocks[0].shape[1]
    out_shape = [jax.ShapeDtypeStruct((rows, matrix.shape[2]), jnp.float32) for matrix in blocks]
    out_shape.append(jax.ShapeDtypeStruct((1, lanes), jnp.float32))
    read = sum(matrix.size * matrix.dtype.itemsize for matrix in blocks)
    outs = pl.pallas_call(
        means_kernel,
        out_shape=out_shape,
        in_specs=[pl.BlockSpec(memory_space=pltpu.VMEM)] * len(blocks),
        out_specs=[pl.BlockSpec(memory_space=pltpu.VMEM)] * len(out_shape),
        cost_estimate=pl.CostEstimate(
            flops=3 * sum(matrix.size for matrix in blocks), transcendentals=0, bytes_accessed=3 * read
        ),
    )(*blocks)
    return list(outs[:-1]), outs[-1].reshape(lanes)


def by_destination(group_means, shard_count):
    rows = group_means[0].shape[0]
    sections = [
        matrix.reshape(rows, shard_count, matrix.shape[-1] // shard_count) for matrix in group_means
    ]
    joined = jnp.concatenate(sections, axis=-1)
    return jnp.transpose(joined, (1, 0, 2)).reshape(shard_count, -1)


def tensor_sum(value):
    count = lax.axis_size("tensor")
    if count == 4:
        masks = (1, 3)
    elif count & (count - 1) == 0:
        masks = tuple(1 << bit for bit in range(count.bit_length() - 1))
    else:
        return lax.psum(value, "tensor")
    for mask in masks:
        pairs = [(index, index ^ mask) for index in range(count)]
        value = value + lax.ppermute(value, "tensor", pairs)
    return value


def shards(
    grad_query,
    grad_key,
    grad_value,
    grad_output,
    grad_gate,
    grad_linear,
    grad_down,
    grad_norms,
    master_flat,
    first_moment,
    second_moment,
    gain_master,
    gain_first,
    gain_second,
):
    blocks = [grad_query, grad_key, grad_value, grad_output, grad_gate, grad_linear, grad_down]
    shard_count = lax.axis_size("shard")
    rows = grad_query.shape[1]
    group_widths = [matrix.shape[2] // shard_count for matrix in blocks]
    flat_width = sum(group_widths)

    lanes = 128
    group_means, block_square = means_and_squares(blocks, lanes)

    gain_local = jnp.sum(grad_norms.astype(jnp.float32), axis=(0, 1))
    gain_size = gain_local.size
    summed = tensor_sum(jnp.concatenate([gain_local.reshape(-1), block_square]))
    gain_grad = summed[:gain_size].reshape(gain_local.shape) * (1.0 / MB)
    gain_square = (gain_grad * gain_grad).reshape(-1)
    shard_square = jnp.sum(
        summed[gain_size:] + jnp.pad(gain_square, (0, lanes - gain_size))
    )

    payload = by_destination(group_means, shard_count)
    payload = jnp.concatenate(
        [payload, jnp.broadcast_to(shard_square, (shard_count, 1))], axis=1
    )
    received = lax.all_to_all(payload, "shard", split_axis=0, concat_axis=0, tiled=True)
    square_total = jnp.sum(received[:, rows * flat_width])
    grad_flat = received[:, : rows * flat_width].reshape(-1)

    grad_rms = jnp.sqrt(square_total / COUNT)
    factor = jnp.minimum(1.0, CLIP_RMS / grad_rms)
    weights, firsts, seconds = adamw(
        master_flat.reshape(-1),
        grad_flat,
        first_moment.reshape(-1),
        second_moment.reshape(-1),
        WDECAY,
        factor,
    )
    gains_new, gain_one, gain_two = adamw(
        gain_master, gain_grad, gain_first, gain_second, 0.0, factor
    )

    lowered = weights.astype(jnp.bfloat16).reshape(shard_count, rows * flat_width)
    returned = lax.all_to_all(lowered, "shard", split_axis=0, concat_axis=0, tiled=True)
    returned = returned.reshape(shard_count, rows, flat_width)
    copies = []
    offset = 0
    for group_width in group_widths:
        section = returned[:, :, offset : offset + group_width]
        copies.append(jnp.transpose(section, (1, 0, 2)).reshape(rows, shard_count * group_width))
        offset = offset + group_width
    gain_copy = gains_new.astype(jnp.bfloat16)
    return (
        weights.reshape(master_flat.shape),
        firsts.reshape(master_flat.shape),
        seconds.reshape(master_flat.shape),
        gains_new,
        gain_one,
        gain_two,
        copies[0],
        copies[1],
        copies[2],
        copies[3],
        copies[4],
        copies[5],
        copies[6],
        gain_copy,
        grad_rms,
    )


def solution(mesh):
    return jax.shard_map(
        shards,
        mesh=mesh,
        in_specs=(
            P(None, "shard", "tensor"),
            P(None, "shard", "tensor"),
            P(None, "shard", "tensor"),
            P(None, "shard", "tensor"),
            P(None, "shard", "tensor"),
            P(None, "shard", "tensor"),
            P(None, "shard", "tensor"),
            P(None, "tensor", None, "shard"),
            P("shard", "tensor", None),
            P("shard", "tensor", None),
            P("shard", "tensor", None),
            P(None, "shard"),
            P(None, "shard"),
            P(None, "shard"),
        ),
        out_specs=(
            P("shard", "tensor", None),
            P("shard", "tensor", None),
            P("shard", "tensor", None),
            P(None, "shard"),
            P(None, "shard"),
            P(None, "shard"),
            P("shard", "tensor"),
            P("shard", "tensor"),
            P("shard", "tensor"),
            P("shard", "tensor"),
            P("shard", "tensor"),
            P("shard", "tensor"),
            P("shard", "tensor"),
            P(None, "shard"),
            P(),
        ),
        check_vma=False,
    )
```

```python
import jax
import jax.numpy as jnp
from jax import lax
from jax.sharding import PartitionSpec as P

MB = 4
STEP = 20
COUNT = 48238592


BETA1 = 0.9
BETA2 = 0.95
EPSILON = 1e-08
LRATE = 0.2
WDECAY = 2.5
CLIP_RMS = 0.5


def adamw(weight, gradient, moment_one, moment_two, decay_rate, factor):
    clipped = gradient * factor
    moment_one_new = BETA1 * moment_one + (1.0 - BETA1) * clipped
    moment_two_new = BETA2 * moment_two + (1.0 - BETA2) * clipped * clipped
    update = (
        moment_one_new
        / (1.0 - BETA1**STEP)
        / (jnp.sqrt(moment_two_new / (1.0 - BETA2**STEP)) + EPSILON)
    )
    return (weight - LRATE * (update + decay_rate * weight), moment_one_new, moment_two_new)


def mean_block(matrix):
    return jnp.sum(matrix.astype(jnp.float32), axis=0) * (1.0 / MB)


def by_destination(group_means, shard_count):
    rows = group_means[0].shape[0]
    sections = [
        matrix.reshape(rows, shard_count, matrix.shape[-1] // shard_count) for matrix in group_means
    ]
    joined = jnp.concatenate(sections, axis=-1)
    return jnp.transpose(joined, (1, 0, 2)).reshape(shard_count, -1)


def tensor_sum(value):
    count = lax.axis_size("tensor")
    index = lax.axis_index("tensor")
    parts = [value]
    for shift in range(1, count):
        pairs = [(source, (source - shift) % count) for source in range(count)]
        parts.append(lax.ppermute(value, "tensor", pairs))
    by_source = jnp.roll(jnp.stack(parts), index, axis=0)
    total = by_source[0]
    for source in range(1, count):
        total = total + by_source[source]
    return total


def shards(
    grad_query,
    grad_key,
    grad_value,
    grad_output,
    grad_gate,
    grad_linear,
    grad_down,
    grad_norms,
    master_flat,
    first_moment,
    second_moment,
    gain_master,
    gain_first,
    gain_second,
):
    blocks = [grad_query, grad_key, grad_value, grad_output, grad_gate, grad_linear, grad_down]
    shard_count = lax.axis_size("shard")
    rows = grad_query.shape[1]
    group_widths = [matrix.shape[2] // shard_count for matrix in blocks]
    flat_width = sum(group_widths)

    group_means = [mean_block(matrix) for matrix in blocks]
    lanes = 128
    block_square = jnp.sum((group_means[0] * group_means[0]).reshape(-1, lanes), axis=0)
    for averaged in group_means[1:]:
        block_square = block_square + jnp.sum((averaged * averaged).reshape(-1, lanes), axis=0)

    gain_local = jnp.sum(grad_norms.astype(jnp.float32), axis=(0, 1))
    gain_size = gain_local.size
    summed = tensor_sum(jnp.concatenate([gain_local.reshape(-1), block_square]))
    gain_grad = summed[:gain_size].reshape(gain_local.shape) * (1.0 / MB)
    gain_square = (gain_grad * gain_grad).reshape(-1)
    shard_square = jnp.sum(
        summed[gain_size:] + jnp.pad(gain_square, (0, lanes - gain_size))
    )

    payload = by_destination(group_means, shard_count)
    payload = jnp.concatenate(
        [payload, jnp.broadcast_to(shard_square, (shard_count, 1))], axis=1
    )
    received = lax.all_to_all(payload, "shard", split_axis=0, concat_axis=0, tiled=True)
    square_total = jnp.sum(received[:, rows * flat_width])
    grad_flat = received[:, : rows * flat_width].reshape(-1)

    grad_rms = jnp.sqrt(square_total / COUNT)
    factor = jnp.minimum(1.0, CLIP_RMS / grad_rms)
    weights, firsts, seconds = adamw(
        master_flat.reshape(-1),
        grad_flat,
        first_moment.reshape(-1),
        second_moment.reshape(-1),
        WDECAY,
        factor,
    )
    gains_new, gain_one, gain_two = adamw(
        gain_master, gain_grad, gain_first, gain_second, 0.0, factor
    )

    lowered = weights.astype(jnp.bfloat16).reshape(shard_count, rows * flat_width)
    returned = lax.all_to_all(lowered, "shard", split_axis=0, concat_axis=0, tiled=True)
    returned = returned.reshape(shard_count, rows, flat_width)
    copies = []
    offset = 0
    for group_width in group_widths:
        section = returned[:, :, offset : offset + group_width]
        copies.append(jnp.transpose(section, (1, 0, 2)).reshape(rows, shard_count * group_width))
        offset = offset + group_width
    gain_copy = gains_new.astype(jnp.bfloat16)
    return (
        weights.reshape(master_flat.shape),
        firsts.reshape(master_flat.shape),
        seconds.reshape(master_flat.shape),
        gains_new,
        gain_one,
        gain_two,
        copies[0],
        copies[1],
        copies[2],
        copies[3],
        copies[4],
        copies[5],
        copies[6],
        gain_copy,
        grad_rms,
    )


def solution(mesh):
    return jax.shard_map(
        shards,
        mesh=mesh,
        in_specs=(
            P(None, "shard", "tensor"),
            P(None, "shard", "tensor"),
            P(None, "shard", "tensor"),
            P(None, "shard", "tensor"),
            P(None, "shard", "tensor"),
            P(None, "shard", "tensor"),
            P(None, "shard", "tensor"),
            P(None, "tensor", None, "shard"),
            P("shard", "tensor", None),
            P("shard", "tensor", None),
            P("shard", "tensor", None),
            P(None, "shard"),
            P(None, "shard"),
            P(None, "shard"),
        ),
        out_specs=(
            P("shard", "tensor", None),
            P("shard", "tensor", None),
            P("shard", "tensor", None),
            P(None, "shard"),
            P(None, "shard"),
            P(None, "shard"),
            P("shard", "tensor"),
            P("shard", "tensor"),
            P("shard", "tensor"),
            P("shard", "tensor"),
            P("shard", "tensor"),
            P("shard", "tensor"),
            P("shard", "tensor"),
            P(None, "shard"),
            P(),
        ),
        check_vma=False,
    )
```

```python
import jax
import jax.numpy as jnp
from jax import lax
from jax.experimental import pallas as pl
from jax.experimental.pallas import tpu as pltpu
from jax.sharding import PartitionSpec as P

MB = 4
STEP = 20
COUNT = 48238592


BETA1 = 0.9
BETA2 = 0.95
EPSILON = 1e-08
LRATE = 0.2
WDECAY = 2.5
CLIP_RMS = 0.5


def adamw(weight, gradient, moment_one, moment_two, decay_rate, factor):
    clipped = gradient * factor
    moment_one_new = BETA1 * moment_one + (1.0 - BETA1) * clipped
    moment_two_new = BETA2 * moment_two + (1.0 - BETA2) * clipped * clipped
    update = (
        moment_one_new
        / (1.0 - BETA1**STEP)
        / (jnp.sqrt(moment_two_new / (1.0 - BETA2**STEP)) + EPSILON)
    )
    return (weight - LRATE * (update + decay_rate * weight), moment_one_new, moment_two_new)


def mean_block(matrix):
    return jnp.sum(matrix.astype(jnp.float32), axis=0) * (1.0 / MB)


def means_kernel(*refs):
    count = (len(refs) - 1) // 2
    grads, means, square_ref = refs[:count], refs[count : 2 * count], refs[2 * count]
    lanes = square_ref.shape[-1]
    square = jnp.zeros((grads[0].shape[1], lanes), jnp.float32)
    for grad_ref, mean_ref in zip(grads, means):
        total = grad_ref[0].astype(jnp.float32)
        for batch in range(1, grad_ref.shape[0]):
            total = total + grad_ref[batch].astype(jnp.float32)
        averaged = total * (1.0 / MB)
        mean_ref[...] = averaged
        for start in range(0, averaged.shape[1], lanes):
            part = averaged[:, start : start + lanes]
            square = square + part * part
    square_ref[...] = jnp.sum(square, axis=0, keepdims=True)


def means_and_squares(blocks, lanes):
    rows = blocks[0].shape[1]
    out_shape = [jax.ShapeDtypeStruct((rows, matrix.shape[2]), jnp.float32) for matrix in blocks]
    out_shape.append(jax.ShapeDtypeStruct((1, lanes), jnp.float32))
    read = sum(matrix.size * matrix.dtype.itemsize for matrix in blocks)
    outs = pl.pallas_call(
        means_kernel,
        out_shape=out_shape,
        in_specs=[pl.BlockSpec(memory_space=pltpu.VMEM)] * len(blocks),
        out_specs=[pl.BlockSpec(memory_space=pltpu.VMEM)] * len(out_shape),
        cost_estimate=pl.CostEstimate(
            flops=3 * sum(matrix.size for matrix in blocks), transcendentals=0, bytes_accessed=3 * read
        ),
    )(*blocks)
    return list(outs[:-1]), outs[-1].reshape(lanes)


def by_destination(group_means, shard_count):
    rows = group_means[0].shape[0]
    sections = [
        matrix.reshape(rows, shard_count, matrix.shape[-1] // shard_count) for matrix in group_means
    ]
    joined = jnp.concatenate(sections, axis=-1)
    return jnp.transpose(joined, (1, 0, 2)).reshape(shard_count, -1)


def tensor_sum(value):
    count = lax.axis_size("tensor")
    index = lax.axis_index("tensor")
    parts = [value]
    for shift in range(1, count):
        pairs = [(source, (source - shift) % count) for source in range(count)]
        parts.append(lax.ppermute(value, "tensor", pairs))
    by_source = jnp.roll(jnp.stack(parts), index, axis=0)
    total = by_source[0]
    for source in range(1, count):
        total = total + by_source[source]
    return total


def shards(
    grad_query,
    grad_key,
    grad_value,
    grad_output,
    grad_gate,
    grad_linear,
    grad_down,
    grad_norms,
    master_flat,
    first_moment,
    second_moment,
    gain_master,
    gain_first,
    gain_second,
):
    blocks = [grad_query, grad_key, grad_value, grad_output, grad_gate, grad_linear, grad_down]
    shard_count = lax.axis_size("shard")
    rows = grad_query.shape[1]
    group_widths = [matrix.shape[2] // shard_count for matrix in blocks]
    flat_width = sum(group_widths)

    lanes = 128
    group_means, block_square = means_and_squares(blocks, lanes)

    gain_local = jnp.sum(grad_norms.astype(jnp.float32), axis=(0, 1))
    gain_size = gain_local.size
    summed = tensor_sum(jnp.concatenate([gain_local.reshape(-1), block_square]))
    gain_grad = summed[:gain_size].reshape(gain_local.shape) * (1.0 / MB)
    gain_square = (gain_grad * gain_grad).reshape(-1)
    shard_square = jnp.sum(
        summed[gain_size:] + jnp.pad(gain_square, (0, lanes - gain_size))
    )

    payload = by_destination(group_means, shard_count)
    payload = jnp.concatenate(
        [payload, jnp.broadcast_to(shard_square, (shard_count, 1))], axis=1
    )
    received = lax.all_to_all(payload, "shard", split_axis=0, concat_axis=0, tiled=True)
    square_total = jnp.sum(received[:, rows * flat_width])
    grad_flat = received[:, : rows * flat_width].reshape(-1)

    grad_rms = jnp.sqrt(square_total / COUNT)
    factor = jnp.minimum(1.0, CLIP_RMS / grad_rms)
    weights, firsts, seconds = adamw(
        master_flat.reshape(-1),
        grad_flat,
        first_moment.reshape(-1),
        second_moment.reshape(-1),
        WDECAY,
        factor,
    )
    gains_new, gain_one, gain_two = adamw(
        gain_master, gain_grad, gain_first, gain_second, 0.0, factor
    )

    lowered = weights.astype(jnp.bfloat16).reshape(shard_count, rows * flat_width)
    returned = lax.all_to_all(lowered, "shard", split_axis=0, concat_axis=0, tiled=True)
    returned = returned.reshape(shard_count, rows, flat_width)
    copies = []
    offset = 0
    for group_width in group_widths:
        section = returned[:, :, offset : offset + group_width]
        copies.append(jnp.transpose(section, (1, 0, 2)).reshape(rows, shard_count * group_width))
        offset = offset + group_width
    gain_copy = gains_new.astype(jnp.bfloat16)
    return (
        weights.reshape(master_flat.shape),
        firsts.reshape(master_flat.shape),
        seconds.reshape(master_flat.shape),
        gains_new,
        gain_one,
        gain_two,
        copies[0],
        copies[1],
        copies[2],
        copies[3],
        copies[4],
        copies[5],
        copies[6],
        gain_copy,
        grad_rms,
    )


def solution(mesh):
    return jax.shard_map(
        shards,
        mesh=mesh,
        in_specs=(
            P(None, "shard", "tensor"),
            P(None, "shard", "tensor"),
            P(None, "shard", "tensor"),
            P(None, "shard", "tensor"),
            P(None, "shard", "tensor"),
            P(None, "shard", "tensor"),
            P(None, "shard", "tensor"),
            P(None, "tensor", None, "shard"),
            P("shard", "tensor", None),
            P("shard", "tensor", None),
            P("shard", "tensor", None),
            P(None, "shard"),
            P(None, "shard"),
            P(None, "shard"),
        ),
        out_specs=(
            P("shard", "tensor", None),
            P("shard", "tensor", None),
            P("shard", "tensor", None),
            P(None, "shard"),
            P(None, "shard"),
            P(None, "shard"),
            P("shard", "tensor"),
            P("shard", "tensor"),
            P("shard", "tensor"),
            P("shard", "tensor"),
            P("shard", "tensor"),
            P("shard", "tensor"),
            P("shard", "tensor"),
            P(None, "shard"),
            P(),
        ),
        check_vma=False,
    )
```

```python
import jax
import jax.numpy as jnp
from jax import lax
from jax.sharding import PartitionSpec as P

MB = 4
STEP = 20
COUNT = 48238592


BETA1 = 0.9
BETA2 = 0.95
EPSILON = 1e-08
LRATE = 0.2
WDECAY = 2.5
CLIP_RMS = 0.5


def adamw(weight, gradient, moment_one, moment_two, decay_rate, factor):
    clipped = gradient * factor
    moment_one_new = BETA1 * moment_one + (1.0 - BETA1) * clipped
    moment_two_new = BETA2 * moment_two + (1.0 - BETA2) * clipped * clipped
    update = (
        moment_one_new
        / (1.0 - BETA1**STEP)
        / (jnp.sqrt(moment_two_new / (1.0 - BETA2**STEP)) + EPSILON)
    )
    return (weight - LRATE * (update + decay_rate * weight), moment_one_new, moment_two_new)


def mean_block(matrix):
    return jnp.sum(matrix.astype(jnp.float32), axis=0) * (1.0 / MB)


def by_destination(group_means, shard_count):
    rows = group_means[0].shape[0]
    sections = [
        matrix.reshape(rows, shard_count, matrix.shape[-1] // shard_count) for matrix in group_means
    ]
    joined = jnp.concatenate(sections, axis=-1)
    return jnp.transpose(joined, (1, 0, 2)).reshape(shard_count, -1)


def tensor_sum(value):
    count = lax.axis_size("tensor")
    if count == 4:
        masks = (1, 3)
    elif count & (count - 1) == 0:
        masks = tuple(1 << bit for bit in range(count.bit_length() - 1))
    else:
        return lax.psum(value, "tensor")
    for mask in masks:
        pairs = [(index, index ^ mask) for index in range(count)]
        value = value + lax.ppermute(value, "tensor", pairs)
    return value


def shards(
    grad_query,
    grad_key,
    grad_value,
    grad_output,
    grad_gate,
    grad_linear,
    grad_down,
    grad_norms,
    master_flat,
    first_moment,
    second_moment,
    gain_master,
    gain_first,
    gain_second,
):
    blocks = [grad_query, grad_key, grad_value, grad_output, grad_gate, grad_linear, grad_down]
    shard_count = lax.axis_size("shard")
    rows = grad_query.shape[1]
    group_widths = [matrix.shape[2] // shard_count for matrix in blocks]
    flat_width = sum(group_widths)

    group_means = [mean_block(matrix) for matrix in blocks]
    lanes = 128
    block_square = jnp.sum((group_means[0] * group_means[0]).reshape(-1, lanes), axis=0)
    for averaged in group_means[1:]:
        block_square = block_square + jnp.sum((averaged * averaged).reshape(-1, lanes), axis=0)

    gain_local = jnp.sum(grad_norms.astype(jnp.float32), axis=(0, 1))
    gain_size = gain_local.size
    summed = tensor_sum(jnp.concatenate([gain_local.reshape(-1), block_square]))
    gain_grad = summed[:gain_size].reshape(gain_local.shape) * (1.0 / MB)
    gain_square = (gain_grad * gain_grad).reshape(-1)
    shard_square = jnp.sum(
        summed[gain_size:] + jnp.pad(gain_square, (0, lanes - gain_size))
    )

    payload = by_destination(group_means, shard_count)
    payload = jnp.concatenate(
        [payload, jnp.broadcast_to(shard_square, (shard_count, 1))], axis=1
    )
    received = lax.all_to_all(payload, "shard", split_axis=0, concat_axis=0, tiled=True)
    square_total = jnp.sum(received[:, rows * flat_width])
    grad_flat = received[:, : rows * flat_width].reshape(-1)

    grad_rms = jnp.sqrt(square_total / COUNT)
    factor = jnp.minimum(1.0, CLIP_RMS / grad_rms)
    weights, firsts, seconds = adamw(
        master_flat.reshape(-1),
        grad_flat,
        first_moment.reshape(-1),
        second_moment.reshape(-1),
        WDECAY,
        factor,
    )
    gains_new, gain_one, gain_two = adamw(
        gain_master, gain_grad, gain_first, gain_second, 0.0, factor
    )

    lowered = weights.astype(jnp.bfloat16)
    returned = lax.all_to_all(lowered, "shard", split_axis=0, concat_axis=0, tiled=True)
    returned = returned.reshape(shard_count, rows, flat_width)
    copies = []
    offset = 0
    for group_width in group_widths:
        section = returned[:, :, offset : offset + group_width]
        copies.append(jnp.transpose(section, (1, 0, 2)).reshape(rows, shard_count * group_width))
        offset = offset + group_width
    gain_copy = gains_new.astype(jnp.bfloat16)
    return (
        weights.reshape(master_flat.shape),
        firsts.reshape(master_flat.shape),
        seconds.reshape(master_flat.shape),
        gains_new,
        gain_one,
        gain_two,
        copies[0],
        copies[1],
        copies[2],
        copies[3],
        copies[4],
        copies[5],
        copies[6],
        gain_copy,
        grad_rms,
    )


def solution(mesh):
    return jax.shard_map(
        shards,
        mesh=mesh,
        in_specs=(
            P(None, "shard", "tensor"),
            P(None, "shard", "tensor"),
            P(None, "shard", "tensor"),
            P(None, "shard", "tensor"),
            P(None, "shard", "tensor"),
            P(None, "shard", "tensor"),
            P(None, "shard", "tensor"),
            P(None, "tensor", None, "shard"),
            P("shard", "tensor", None),
            P("shard", "tensor", None),
            P("shard", "tensor", None),
            P(None, "shard"),
            P(None, "shard"),
            P(None, "shard"),
        ),
        out_specs=(
            P("shard", "tensor", None),
            P("shard", "tensor", None),
            P("shard", "tensor", None),
            P(None, "shard"),
            P(None, "shard"),
            P(None, "shard"),
            P("shard", "tensor"),
            P("shard", "tensor"),
            P("shard", "tensor"),
            P("shard", "tensor"),
            P("shard", "tensor"),
            P("shard", "tensor"),
            P("shard", "tensor"),
            P(None, "shard"),
            P(),
        ),
        check_vma=False,
    )
```
